32 devices in a mesh: frames: 2 (over x), lenslet: 16 (over z, y, core).
Axes of the slice: x: 2, y: 2, z: 4, core: 2. Of those that a mesh axis runs over, the one named last changes fastest.
Arguments:
- volume: bfloat16 [8, 256, 64, 400], P('frames', 'lenslet'), parts along dimension 0, may hold values from 0.099609375 to 1
- measured: float32 [512, 64, 400], P(('frames', 'lenslet')), parts along dimension 0, may hold values from 0.2 to 2
- operator_rows: bfloat16 [12800, 400], P('lenslet'), may hold values from 2.9831426e-10 to 0.0029907227
- offset_counts: int32 [4], replicated, may hold values from 1 to 25, 32 in all
- offset_table: int32 [32, 2], replicated, may hold values from -2 to 2
- dark_level: float32 [400], replicated, may hold values from 0.2 to 1
Outputs:
- predicted: float32 [512, 64, 400], P(('frames', 'lenslet')), parts along dimension 0
- ratio: float32 [512, 64, 400], P(('frames', 'lenslet')), parts along dimension 0
The draws below stay inside these ranges and needn't reach their ends.
There are 2 independent parts, one for each index of `frames`. The reference program is written for one: setup_inputs(seed, part) draws one part's arguments, and reference() takes and returns one part's arrays. A program takes and returns all parts, laid end to end along the dimension named above; an argument that names none is the same for every part. Nothing has to cross between parts.
Inputs may be any that keep to these rules, and one draw needn't show every extreme that they name: `offset_counts`: counts sum to 32.
All inputs are finite; a program needn't handle non-finite values.
Results may differ from the reference program's by a relative error of at most 0.0003.
Values may be sent and summed in bfloat16 or wider, within the bound.
No kernel may reach another device: no remote copies, remote signals or barrier semaphores. Data moves between devices by JAX's collectives and lax.ppermute only.
A program may use at most 192 MiB of HBM per device.

```python
import math
import jax
import jax.numpy as jnp
import numpy as np
from jax import lax

PIX = 400
LX = 64
DEPTHS = 4
NOPS = 32
MOST_OFFSETS = 25
REACH = 2
ROWS = 256


def place_ends(values, own_key, least, high):
    spot = [jax.random.randint(jax.random.fold_in(own_key, axis), (), 0, length) for axis, length in enumerate(values.shape)]
    longest = values.shape.index(max(values.shape))
    beside = spot[:longest] + [(spot[longest] + 1) % values.shape[longest]] + spot[longest + 1:]
    return values.at[tuple(spot)].set(least).at[tuple(beside)].set(high)


def levels(own_key, dims, pieces, least, high):
    def one(position, parts):
        draws = jax.random.uniform(jax.random.fold_in(jax.random.fold_in(own_key, 6), position), (parts,), jnp.float32, least / len(pieces), high / len(pieces))
        return jnp.repeat(jnp.exp(draws), dims[position] // parts).reshape((-1,) + (1,) * (len(dims) - position - 1))

    loudness = one(*pieces[0])
    for cut in pieces[1:]:
        loudness = loudness * one(*cut)
    return loudness


def length_profile(count, total, limit, skew):
    loads = [(1 << 20) // math.isqrt(grade ** skew) + 1 for grade in range(2, count + 1)]
    surplus, given = total - limit - (count - 1), [1] * (count - 1)
    while surplus > 0:
        candidates = [i for i in range(count - 1) if given[i] < limit]
        whole, left = sum([loads[i] for i in candidates]), surplus
        for i in candidates:
            addition = min(limit - given[i], max(1, left * loads[i] // whole), surplus)
            given[i] = given[i] + addition
            surplus = surplus - addition
    return np.array([limit] + given)


def ragged_sizes(rng, count, total, reach, slope):
    if count == 2:
        one = jax.random.randint(rng, (), max(1, total - reach), min(reach, total - 1) + 1)
        return jnp.stack([one, total - one])
    sizes = jnp.asarray(length_profile(count, total, reach, slope), jnp.int32)
    twos = (count - 1) // 2
    giver, taker = sizes[1:1 + 2 * twos:2], sizes[2:2 + 2 * twos:2]
    margin = jnp.minimum(giver - 1, reach - taker)
    shifted = jax.random.randint(jax.random.fold_in(rng, 1), (twos,), 0, 1 << 20) % (margin + 1)
    sizes = sizes.at[1:1 + 2 * twos:2].set(giver - shifted).at[2:2 + 2 * twos:2].set(taker + shifted)
    return sizes[jax.random.permutation(jax.random.fold_in(rng, 2), count)]


def setup_inputs(seed: int = 0, part: int = 0) -> dict:
    key_list = jax.random.split(jax.random.key(seed), 7)
    part_keys = jax.random.split(jax.random.fold_in(key_list[6], part), 7)
    volume = jnp.clip(jnp.exp(math.log(1.0) - 2.306499 * jax.random.uniform(part_keys[0], (DEPTHS, ROWS, LX, PIX), jnp.float32) ** levels(part_keys[0], (DEPTHS, ROWS, LX, PIX), ((1, 16),), -0.2, 0.2)), 0.099609375, 1.0).astype(jnp.bfloat16)
    measured = jnp.clip(jnp.exp(math.log(2.0) - 2.3025851 * jax.random.uniform(part_keys[1], (ROWS, LX, PIX), jnp.float32) ** levels(part_keys[1], (ROWS, LX, PIX), ((0, 16),), -0.2, 0.2)), 0.2, 2.0)
    operator_rows = jnp.clip(jnp.exp(math.log(0.0029907227) - 16.1206334 * jax.random.uniform(key_list[2], (NOPS * PIX, PIX), jnp.float32) ** levels(key_list[2], (NOPS * PIX, PIX), ((0, 16),), -0.2, 0.2)), 2.9831426218152046e-10, 0.0029907227).astype(jnp.bfloat16)
    offset_counts = ragged_sizes(key_list[3], DEPTHS, NOPS, MOST_OFFSETS, 0).astype(jnp.int32)
    offset_table = place_ends(jax.random.randint(key_list[4], (NOPS, 2), -2, 3), jax.random.fold_in(key_list[4], 1), -2, 2).astype(jnp.int32)
    dark_level = jnp.clip(jnp.exp(jax.random.uniform(key_list[5], (PIX,), jnp.float32, math.log(0.2), math.log(1.0))), 0.2, 1.0)
    return {"volume": volume, "measured": measured, "operator_rows": operator_rows, "offset_counts": offset_counts, "offset_table": offset_table, "dark_level": dark_level}


def reference(volume, measured, operator_rows, offset_counts, offset_table, dark_level):
    padded = jnp.pad(volume, ((0, 0), (REACH, REACH), (REACH, REACH), (0, 0)))
    ends = jnp.cumsum(offset_counts).astype(jnp.int32)
    positions = jnp.arange(NOPS, dtype=jnp.int32)
    depth_of = jnp.sum((positions[:, None] >= ends[None, :]).astype(jnp.int32), axis=1).astype(jnp.int32)

    def accumulate(index, total):
        index = jnp.asarray(index).astype(jnp.int32)
        start_row = (offset_table[index, 0] + REACH).astype(jnp.int32)
        start_col = (offset_table[index, 1] + REACH).astype(jnp.int32)
        slab = lax.dynamic_slice(padded, (depth_of[index], start_row, start_col, jnp.int32(0)), (1, ROWS, LX, PIX))
        slab = slab.reshape(ROWS * LX, PIX)
        block = lax.dynamic_slice_in_dim(operator_rows, (index * PIX).astype(jnp.int32), PIX, 0)
        return total + jnp.dot(slab, block, preferred_element_type=jnp.float32)

    total = lax.fori_loop(0, NOPS, accumulate, jnp.zeros((ROWS * LX, PIX), jnp.float32))
    predicted = total.reshape(ROWS, LX, PIX)
    ratio = measured / (predicted + dark_level)
    return (predicted, ratio)
```

```python
import jax
import jax.numpy as jnp
from jax import lax
from jax.experimental import pallas as pl
from jax.experimental.pallas import tpu as pltpu
from jax.sharding import PartitionSpec as P

REACH = 2


def passed_along(block, axis, distance):
    devices = range(lax.axis_size(axis))
    route = [(i - distance, i) for i in devices if i - distance in devices]
    return lax.ppermute(block, axis, route)


def project_kernel(depth_ref, row_ref, col_ref, vol_ref, op_ref, meas_ref, dark_ref, pred_ref, ratio_ref):
    k = pl.program_id(0)
    _, _, _, columns, pixels = vol_ref.shape
    rows = pred_ref.shape[0] // columns

    @pl.when(k == 0)
    def _():
        pred_ref[...] = jnp.zeros_like(pred_ref)

    slab = vol_ref[col_ref[k], depth_ref[k], pl.ds(row_ref[k], rows), :, :]
    slab = slab.reshape(rows * columns, pixels)
    pred_ref[...] += jnp.dot(slab, op_ref[...], preferred_element_type=jnp.float32)

    @pl.when(k == pl.num_programs(0) - 1)
    def _():
        ratio_ref[...] = meas_ref[...] / (pred_ref[...] + dark_ref[...])


def body(volume, measured, operator_rows, offset_counts, offset_table, dark_level):
    depths, rows_here, columns, pixels = volume.shape
    op_total = offset_table.shape[0]
    ends = jnp.cumsum(offset_counts)
    positions = jnp.arange(op_total, dtype=jnp.int32)
    depth_of = jnp.sum((positions[:, None] >= ends[None, :]).astype(jnp.int32), axis=1)
    row_start = (offset_table[:, 0] + REACH).astype(jnp.int32)
    col_start = (offset_table[:, 1] + REACH).astype(jnp.int32)
    above = passed_along(volume[:, rows_here - REACH :], "lenslet", 1)
    below = passed_along(volume[:, :REACH], "lenslet", -1)
    extended = jnp.concatenate([above, volume, below], axis=1)
    extended = jnp.pad(extended, ((0, 0), (0, 0), (REACH, REACH), (0, 0)))
    shifted = jnp.stack([extended[:, :, s : s + columns] for s in range(2 * REACH + 1)])
    operators = lax.all_gather(operator_rows, "lenslet", axis=0, tiled=True)
    image_rows = rows_here * columns
    flat = lambda k, *_: (0, 0)
    predicted, ratio = pl.pallas_call(
        project_kernel,
        grid_spec=pltpu.PrefetchScalarGridSpec(
            num_scalar_prefetch=3,
            grid=(op_total,),
            in_specs=[
                pl.BlockSpec(memory_space=pltpu.VMEM),
                pl.BlockSpec((pixels, pixels), lambda k, *_: (k, 0)),
                pl.BlockSpec((image_rows, pixels), flat),
                pl.BlockSpec((1, pixels), flat),
            ],
            out_specs=[
                pl.BlockSpec((image_rows, pixels), flat),
                pl.BlockSpec((image_rows, pixels), flat),
            ],
        ),
        out_shape=[
            jax.ShapeDtypeStruct((image_rows, pixels), jnp.float32),
            jax.ShapeDtypeStruct((image_rows, pixels), jnp.float32),
        ],
        compiler_params=pltpu.CompilerParams(dimension_semantics=("arbitrary",)),
    )(
        depth_of,
        row_start,
        col_start,
        shifted,
        operators,
        measured.reshape(image_rows, pixels),
        dark_level.reshape(1, pixels),
    )
    return (predicted.reshape(rows_here, columns, pixels), ratio.reshape(rows_here, columns, pixels))


def solution(mesh):
    placed = (
        P("frames", "lenslet", None, None),
        P(("frames", "lenslet"), None, None),
        P("lenslet", None),
        P(),
        P(),
        P(),
    )
    return jax.shard_map(
        body,
        mesh=mesh,
        in_specs=placed,
        out_specs=(P(("frames", "lenslet"), None, None), P(("frames", "lenslet"), None, None)),
        check_vma=False,
    )
```
